128 devices in a mesh: row: 8 (over y, z_hi), col: 16 (over z_lo, x, core).
Axes of the slice: x: 4, y: 4, z: 4 (z_hi: 2, z_lo: 2; z = z_hi * 2 + z_lo), core: 2. Of those that a mesh axis runs over, the one named last changes fastest.
Arguments:
- upper_stored: bfloat16 [6144, 6144], P('row', 'col'), may hold values from -6 to 6
- block_cells: int32 [96, 3], replicated, may hold values from 0 to 15
Outputs:
- purified: bfloat16 [6144, 6144], P('row', 'col')
The draws below stay inside these ranges and needn't reach their ends.
Inputs may be any that keep to these rules, and one draw needn't show every extreme that they name: `block_cells`: integer cell coordinates of each atom block on a periodic lattice of 16 cells a side.
All inputs are finite; a program needn't handle non-finite values.
Results may differ from the reference program's by a relative error of at most 0.0067.
Values may be sent and summed in bfloat16 or wider, within the bound.
No kernel may reach another device: no remote copies, remote signals or barrier semaphores. Data moves between devices by JAX's collectives and lax.ppermute only.
A program may use at most 64 MiB of HBM per device.

```python
import math
import jax
import jax.numpy as jnp
from jax import lax

BLK = 64
BOX = 16
NEAR = 40
FAR = 90
NB = 96
N = 6144


def touch_ends(entries, stream_key, low, largest):
    dims = entries.shape
    place = [jax.random.randint(jax.random.fold_in(stream_key, axis), (), 0, dims[axis]) for axis in range(len(dims))]
    entries = entries.at[tuple(place)].set(low)
    longest = dims.index(max(dims))
    place[longest] = (place[longest] + 1) % dims[longest]
    return entries.at[tuple(place)].set(largest)


def block_scale(stream_key, dims, cuts, least, top_value):
    def one(position, blocks):
        draws = jax.random.uniform(jax.random.fold_in(jax.random.fold_in(stream_key, 6), position), (blocks,), jnp.float32, least / len(cuts), top_value / len(cuts))
        return jnp.repeat(jnp.exp(draws), dims[position] // blocks).reshape((-1,) + (1,) * (len(dims) - position - 1))

    gain = one(*cuts[0])
    for cut in cuts[1:]:
        gain = gain * one(*cut)
    return gain


def scatter_about(rng, extent, scale, reach, split=(), kind=jnp.bfloat16):
    array = scale * jax.random.normal(rng, extent, jnp.float32)
    if split:
        array = array * block_scale(rng, extent, split, -0.22, 0.18)
    return jnp.clip(array, -reach, reach).astype(kind)


def setup_inputs(seed: int = 0) -> dict:
    splits = jax.random.split(jax.random.key(seed), 3)
    return {
        "upper_stored": scatter_about(splits[0], (N, N), 1.0, 6.0, ((0, 8), (1, 16))),
        "block_cells": touch_ends(jax.random.randint(splits[1], (NB, 3), 0, BOX), jax.random.fold_in(splits[1], 1), 0, BOX - 1).astype(jnp.int32),
    }


def cell_mask(block_cells, bound_sq):
    offset_abs = jnp.abs(block_cells[:, None, :] - block_cells[None, :, :])
    wrapped = jnp.minimum(offset_abs, BOX - offset_abs)
    return lax.optimization_barrier(jnp.sum(wrapped * wrapped, axis=2)) <= bound_sq

def expand_mask(keep_mask):
    return jnp.repeat(jnp.repeat(keep_mask, BLK, axis=0), BLK, axis=1)

def reference(upper_stored, block_cells):
    order_total = upper_stored.shape[0]
    index_rows = lax.broadcasted_iota(jnp.int32, (order_total, order_total), 0)
    index_cols = lax.broadcasted_iota(jnp.int32, (order_total, order_total), 1)
    symmetric = jnp.where(index_rows <= index_cols, upper_stored, upper_stored.T)
    near_keep = expand_mask(cell_mask(block_cells, NEAR))
    far_keep = expand_mask(cell_mask(block_cells, FAR))
    diagonal = jnp.where(index_rows == index_cols, 0.5, 0.0).astype(jnp.float32)
    value_scale = 2.0 / math.sqrt(order_total)
    density_full = diagonal + value_scale * symmetric.astype(jnp.float32)
    density = jnp.where(near_keep, density_full, jnp.zeros_like(density_full)).astype(jnp.bfloat16)
    product = jnp.dot(density, density, preferred_element_type=jnp.float32)
    square = jnp.where(far_keep, product, jnp.zeros_like(product))
    square_low = square.astype(jnp.bfloat16)
    cubic = jnp.dot(square_low, density, preferred_element_type=jnp.float32)
    result = 3.0 * square - 2.0 * cubic
    return jnp.where(near_keep, result, jnp.zeros_like(result)).astype(jnp.bfloat16)
```

```python
import math

import jax
import jax.numpy as jnp
from jax import lax
from jax.sharding import PartitionSpec as P

BLK = 64
BOX = 16
NEAR = 40
FAR = 90


def cell_mask(block_cells, row_start, row_count, col_start, col_count, bound_sq):
    row_cells = lax.dynamic_slice_in_dim(block_cells, row_start, row_count, 0)
    col_cells = lax.dynamic_slice_in_dim(block_cells, col_start, col_count, 0)
    offset_abs = jnp.abs(row_cells[:, None, :] - col_cells[None, :, :])
    wrapped = jnp.minimum(offset_abs, BOX - offset_abs)
    return jnp.sum(wrapped * wrapped, axis=2) <= bound_sq


def block_keep(matrix_tile, keep_mask):
    row_count, col_count = matrix_tile.shape
    row_blocks, col_blocks = keep_mask.shape
    shaped = matrix_tile.reshape(
        row_blocks, row_count // row_blocks, col_blocks, col_count // col_blocks
    )
    kept = jnp.where(keep_mask[:, None, :, None], shaped, jnp.zeros_like(shaped))
    return kept.reshape(row_count, col_count)


def mirror_tile(upper_stored, rows, cols):
    tile_side, half_width = upper_stored.shape
    row_id = lax.axis_index("row")
    col_id = lax.axis_index("col")
    pieces = []
    for k in range(2):
        half = (col_id + k) % 2
        piece = lax.dynamic_slice_in_dim(upper_stored, half * half_width, half_width, 0)
        pairs = []
        for a in range(rows):
            for b in range(cols):
                h = (b + k) % 2
                pairs.append((a * cols + b, (b // 2) * cols + 2 * a + h))
        pieces.append(lax.ppermute(piece, ("row", "col"), pairs))
    h_own = col_id % 2
    first = jnp.where(h_own == 0, pieces[0], pieces[1])
    second = jnp.where(h_own == 0, pieces[1], pieces[0])
    return jnp.concatenate([first, second], 1).T


def per_device(upper_stored, block_cells):
    rows = lax.axis_size("row")
    cols = lax.axis_size("col")
    row_id = lax.axis_index("row")
    col_id = lax.axis_index("col")
    tile_side, half_width = upper_stored.shape
    order_total = tile_side * rows
    tile_blocks = tile_side // BLK
    half_blocks = half_width // BLK
    mirrored = mirror_tile(upper_stored, rows, cols)
    global_rows = row_id * tile_side + lax.broadcasted_iota(jnp.int32, (tile_side, half_width), 0)
    global_cols = col_id * half_width + lax.broadcasted_iota(jnp.int32, (tile_side, half_width), 1)
    symmetric = jnp.where(global_rows <= global_cols, upper_stored, mirrored)
    near_own = cell_mask(
        block_cells, row_id * tile_blocks, tile_blocks, col_id * half_blocks, half_blocks, NEAR
    )
    far_own = cell_mask(
        block_cells, row_id * tile_blocks, tile_blocks, col_id * half_blocks, half_blocks, FAR
    )
    diagonal = jnp.where(global_rows == global_cols, 0.5, 0.0).astype(jnp.float32)
    value_scale = 2.0 / math.sqrt(order_total)
    density = block_keep(
        diagonal + value_scale * symmetric.astype(jnp.float32), near_own
    ).astype(jnp.bfloat16)
    row_panel = lax.all_gather(density, "col", axis=1, tiled=True)
    col_panel = lax.all_gather(density, "row", axis=0, tiled=True)
    square = block_keep(
        jnp.dot(row_panel, col_panel, preferred_element_type=jnp.float32), far_own
    )
    square_low = square.astype(jnp.bfloat16)
    low_panel = lax.all_gather(square_low, "col", axis=1, tiled=True)
    cubic = jnp.dot(low_panel, col_panel, preferred_element_type=jnp.float32)
    return block_keep(3.0 * square - 2.0 * cubic, near_own).astype(jnp.bfloat16)


def solution(mesh):
    return jax.shard_map(
        per_device,
        mesh=mesh,
        in_specs=(P("row", "col"), P()),
        out_specs=P("row", "col"),
        check_vma=False,
    )
```

```python
import math

import jax
import jax.numpy as jnp
from jax import lax
from jax.sharding import Mesh
from jax.sharding import PartitionSpec as P

BLK = 64
BOX = 16
NEAR = 40
FAR = 90


def cell_mask(block_cells, row_start, row_count, col_start, col_count, bound_sq):
    row_cells = lax.dynamic_slice_in_dim(block_cells, row_start, row_count, 0)
    col_cells = lax.dynamic_slice_in_dim(block_cells, col_start, col_count, 0)
    offset_abs = jnp.abs(row_cells[:, None, :] - col_cells[None, :, :])
    wrapped = jnp.minimum(offset_abs, BOX - offset_abs)
    return jnp.sum(wrapped * wrapped, axis=2) <= bound_sq


def block_keep(matrix_tile, keep_mask):
    row_count, col_count = matrix_tile.shape
    row_blocks, col_blocks = keep_mask.shape
    shaped = matrix_tile.reshape(
        row_blocks, row_count // row_blocks, col_blocks, col_count // col_blocks
    )
    kept = jnp.where(keep_mask[:, None, :, None], shaped, jnp.zeros_like(shaped))
    return kept.reshape(row_count, col_count)


ROW = ("y", "zh")
COL = ("zl", "x", "core")


def column_panel(tile):
    partner = lax.ppermute(tile, "zh", [(0, 1), (1, 0)])
    zh_id = lax.axis_index("zh")
    pair = jnp.where(zh_id == 0, jnp.concatenate([tile, partner], 0), jnp.concatenate([partner, tile], 0))
    ring = lax.axis_size("y")
    from_below = lax.ppermute(pair, "y", [(i, (i + 1) % ring) for i in range(ring)])
    from_above = lax.ppermute(pair, "y", [(i, (i - 1) % ring) for i in range(ring)])
    from_two_below = lax.ppermute(from_below, "y", [(i, (i + 1) % ring) for i in range(ring)])
    y_id = lax.axis_index("y")
    panel = jnp.zeros((ring,) + pair.shape, pair.dtype)
    for offset, part in ((0, pair), (-1, from_below), (-2, from_two_below), (1, from_above)):
        panel = lax.dynamic_update_index_in_dim(panel, part, (y_id + offset) % ring, 0)
    return panel.reshape(ring * pair.shape[0], pair.shape[1])


def mirror_tile(upper_stored, rows, cols):
    tile_side, half_width = upper_stored.shape
    row_id = lax.axis_index(ROW)
    col_id = lax.axis_index(COL)
    pieces = []
    for k in range(2):
        half = (col_id + k) % 2
        piece = lax.dynamic_slice_in_dim(upper_stored, half * half_width, half_width, 0)
        pairs = []
        for a in range(rows):
            for b in range(cols):
                h = (b + k) % 2
                pairs.append((a * cols + b, (b // 2) * cols + 2 * a + h))
        pieces.append(lax.ppermute(piece, ROW + COL, pairs))
    h_own = col_id % 2
    first = jnp.where(h_own == 0, pieces[0], pieces[1])
    second = jnp.where(h_own == 0, pieces[1], pieces[0])
    return jnp.concatenate([first, second], 1).T


def per_device(upper_stored, block_cells):
    rows = lax.axis_size(ROW)
    cols = lax.axis_size(COL)
    row_id = lax.axis_index(ROW)
    col_id = lax.axis_index(COL)
    tile_side, half_width = upper_stored.shape
    order_total = tile_side * rows
    tile_blocks = tile_side // BLK
    half_blocks = half_width // BLK
    mirrored = mirror_tile(upper_stored, rows, cols)
    global_rows = row_id * tile_side + lax.broadcasted_iota(jnp.int32, (tile_side, half_width), 0)
    global_cols = col_id * half_width + lax.broadcasted_iota(jnp.int32, (tile_side, half_width), 1)
    symmetric = jnp.where(global_rows <= global_cols, upper_stored, mirrored)
    near_own = cell_mask(
        block_cells, row_id * tile_blocks, tile_blocks, col_id * half_blocks, half_blocks, NEAR
    )
    far_own = cell_mask(
        block_cells, row_id * tile_blocks, tile_blocks, col_id * half_blocks, half_blocks, FAR
    )
    diagonal = jnp.where(global_rows == global_cols, 0.5, 0.0).astype(jnp.float32)
    value_scale = 2.0 / math.sqrt(order_total)
    density = block_keep(
        diagonal + value_scale * symmetric.astype(jnp.float32), near_own
    ).astype(jnp.bfloat16)
    row_panel = lax.all_gather(density, COL, axis=1, tiled=True)
    col_panel = column_panel(density)
    square = block_keep(
        jnp.dot(row_panel, col_panel, preferred_element_type=jnp.float32), far_own
    )
    square_low = square.astype(jnp.bfloat16)
    low_panel = lax.all_gather(square_low, COL, axis=1, tiled=True)
    cubic = jnp.dot(low_panel, col_panel, preferred_element_type=jnp.float32)
    return block_keep(3.0 * square - 2.0 * cubic, near_own).astype(jnp.bfloat16)


def solution(mesh):
    y_size = mesh.devices.shape[0] // 2
    x_size = mesh.devices.shape[1] // 4
    split_mesh = Mesh(mesh.devices.reshape(y_size, 2, 2, x_size, 2), ROW + COL)
    return jax.shard_map(
        per_device,
        mesh=split_mesh,
        in_specs=(P(ROW, COL), P()),
        out_specs=P(ROW, COL),
        check_vma=False,
    )
```

```python
import math

import jax
import jax.numpy as jnp
from jax import lax
from jax.sharding import Mesh
from jax.sharding import PartitionSpec as P

BLK = 64
BOX = 16
NEAR = 40
FAR = 90
ROW = ("y", "zh")
COL = ("zl", "x", "core")
CHUNKS = 4


def cell_mask(block_cells, row_start, row_count, col_start, col_count, bound_sq):
    row_cells = lax.dynamic_slice_in_dim(block_cells, row_start, row_count, 0)
    col_cells = lax.dynamic_slice_in_dim(block_cells, col_start, col_count, 0)
    offset_abs = jnp.abs(row_cells[:, None, :] - col_cells[None, :, :])
    wrapped = jnp.minimum(offset_abs, BOX - offset_abs)
    keep = jnp.sum(wrapped * wrapped, axis=2) <= bound_sq
    return jnp.repeat(jnp.repeat(keep, BLK, axis=0), BLK, axis=1)


def chunked_shift(value, axis, pairs):
    step = value.shape[0] // CHUNKS
    parts = [lax.ppermute(value[i * step:(i + 1) * step], axis, pairs) for i in range(CHUNKS)]
    return jnp.concatenate(parts, 0)


def column_panel_t(tile_t):
    partner = chunked_shift(tile_t, "zh", [(0, 1), (1, 0)])
    zh_id = lax.axis_index("zh")
    pair = jnp.where(zh_id == 0, jnp.concatenate([tile_t, partner], 1), jnp.concatenate([partner, tile_t], 1))
    ring = lax.axis_size("y")
    up = [(i, (i + 1) % ring) for i in range(ring)]
    down = [(i, (i - 1) % ring) for i in range(ring)]
    from_below = chunked_shift(pair, "y", up)
    from_above = chunked_shift(pair, "y", down)
    from_two_below = chunked_shift(from_below, "y", up)
    y_id = lax.axis_index("y")
    width = pair.shape[1]
    panel = jnp.zeros((pair.shape[0], ring * width), pair.dtype)
    for offset, part in ((0, pair), (-1, from_below), (-2, from_two_below), (1, from_above)):
        panel = lax.dynamic_update_slice_in_dim(panel, part, ((y_id + offset) % ring) * width, 1)
    return panel


def mirror_tile(upper_stored, rows, cols):
    tile_side, half_width = upper_stored.shape
    col_id = lax.axis_index(COL)
    pieces = []
    for k in range(2):
        half = (col_id + k) % 2
        piece = lax.dynamic_slice_in_dim(upper_stored, half * half_width, half_width, 0)
        pairs = []
        for a in range(rows):
            for b in range(cols):
                h = (b + k) % 2
                pairs.append((a * cols + b, (b // 2) * cols + 2 * a + h))
        pieces.append(lax.ppermute(piece, ROW + COL, pairs))
    h_own = col_id % 2
    first = jnp.where(h_own == 0, pieces[0], pieces[1])
    second = jnp.where(h_own == 0, pieces[1], pieces[0])
    return jnp.concatenate([first, second], 1).T


def dot_t(left, right_t):
    return lax.dot_general(left, right_t, (((1,), (1,)), ((), ())), preferred_element_type=jnp.float32)


def per_device(upper_stored, block_cells):
    rows = lax.axis_size(ROW)
    cols = lax.axis_size(COL)
    row_id = lax.axis_index(ROW)
    col_id = lax.axis_index(COL)
    tile_side, half_width = upper_stored.shape
    order_total = tile_side * rows
    tile_blocks = tile_side // BLK
    half_blocks = half_width // BLK
    mirrored = mirror_tile(upper_stored, rows, cols)
    global_rows = row_id * tile_side + lax.broadcasted_iota(jnp.int32, (tile_side, half_width), 0)
    global_cols = col_id * half_width + lax.broadcasted_iota(jnp.int32, (tile_side, half_width), 1)
    symmetric = jnp.where(global_rows <= global_cols, upper_stored, mirrored)
    near_own = cell_mask(
        block_cells, row_id * tile_blocks, tile_blocks, col_id * half_blocks, half_blocks, NEAR
    )
    far_own = cell_mask(
        block_cells, row_id * tile_blocks, tile_blocks, col_id * half_blocks, half_blocks, FAR
    )
    diagonal = jnp.where(global_rows == global_cols, 0.5, 0.0).astype(jnp.float32)
    value_scale = 2.0 / math.sqrt(order_total)
    density_full = diagonal + value_scale * symmetric.astype(jnp.float32)
    density = jnp.where(near_own, density_full, 0.0).astype(jnp.bfloat16)
    row_panel = lax.all_gather(density, COL, axis=1, tiled=True)
    col_panel_t = column_panel_t(density.T)
    square = jnp.where(far_own, dot_t(row_panel, col_panel_t), 0.0)
    square_low = square.astype(jnp.bfloat16)
    low_panel = lax.all_gather(square_low, COL, axis=1, tiled=True)
    cubic = dot_t(low_panel, col_panel_t)
    return jnp.where(near_own, 3.0 * square - 2.0 * cubic, 0.0).astype(jnp.bfloat16)


def solution(mesh):
    y_size = mesh.devices.shape[0] // 2
    x_size = mesh.devices.shape[1] // 4
    split_mesh = Mesh(mesh.devices.reshape(y_size, 2, 2, x_size, 2), ROW + COL)
    return jax.shard_map(
        per_device,
        mesh=split_mesh,
        in_specs=(P(ROW, COL), P()),
        out_specs=P(ROW, COL),
        check_vma=False,
    )
```

```python
import math

import jax
import jax.numpy as jnp
from jax import lax
from jax.sharding import Mesh
from jax.sharding import PartitionSpec as P

BLK = 64
BOX = 16
NEAR = 40
FAR = 90
ROW = ("y", "zh")
COL = ("zl", "x", "core")
CHUNKS = 1


def cell_mask(block_cells, row_start, row_count, col_start, col_count, bound_sq):
    row_cells = lax.dynamic_slice_in_dim(block_cells, row_start, row_count, 0)
    col_cells = lax.dynamic_slice_in_dim(block_cells, col_start, col_count, 0)
    offset_abs = jnp.abs(row_cells[:, None, :] - col_cells[None, :, :])
    wrapped = jnp.minimum(offset_abs, BOX - offset_abs)
    keep = jnp.sum(wrapped * wrapped, axis=2) <= bound_sq
    return jnp.repeat(jnp.repeat(keep, BLK, axis=0), BLK, axis=1)


def chunked_shift(value, axis, pairs):
    step = value.shape[0] // CHUNKS
    parts = [lax.ppermute(value[i * step:(i + 1) * step], axis, pairs) for i in range(CHUNKS)]
    return jnp.concatenate(parts, 0)


def column_panel_t(tile_t):
    partner = chunked_shift(tile_t, "zh", [(0, 1), (1, 0)])
    zh_id = lax.axis_index("zh")
    pair = jnp.where(zh_id == 0, jnp.concatenate([tile_t, partner], 1), jnp.concatenate([partner, tile_t], 1))
    ring = lax.axis_size("y")
    up = [(i, (i + 1) % ring) for i in range(ring)]
    down = [(i, (i - 1) % ring) for i in range(ring)]
    from_below = chunked_shift(pair, "y", up)
    from_above = chunked_shift(pair, "y", down)
    from_two_below = chunked_shift(from_below, "y", up)
    y_id = lax.axis_index("y")
    width = pair.shape[1]
    panel = jnp.zeros((pair.shape[0], ring * width), pair.dtype)
    for offset, part in ((0, pair), (-1, from_below), (-2, from_two_below), (1, from_above)):
        panel = lax.dynamic_update_slice_in_dim(panel, part, ((y_id + offset) % ring) * width, 1)
    return panel


def mirror_tile(upper_stored, rows, cols):
    tile_side, half_width = upper_stored.shape
    col_id = lax.axis_index(COL)
    pieces = []
    for k in range(2):
        half = (col_id + k) % 2
        piece = lax.dynamic_slice_in_dim(upper_stored, half * half_width, half_width, 0)
        pairs = []
        for a in range(rows):
            for b in range(cols):
                h = (b + k) % 2
                pairs.append((a * cols + b, (b // 2) * cols + 2 * a + h))
        pieces.append(lax.ppermute(piece, ROW + COL, pairs))
    h_own = col_id % 2
    first = jnp.where(h_own == 0, pieces[0], pieces[1])
    second = jnp.where(h_own == 0, pieces[1], pieces[0])
    return jnp.concatenate([first, second], 1).T


def dot_t(left, right_t):
    return lax.dot_general(left, right_t, (((1,), (1,)), ((), ())), preferred_element_type=jnp.float32)


def per_device(upper_stored, block_cells):
    rows = lax.axis_size(ROW)
    cols = lax.axis_size(COL)
    row_id = lax.axis_index(ROW)
    col_id = lax.axis_index(COL)
    tile_side, half_width = upper_stored.shape
    order_total = tile_side * rows
    tile_blocks = tile_side // BLK
    half_blocks = half_width // BLK
    mirrored = mirror_tile(upper_stored, rows, cols)
    global_rows = row_id * tile_side + lax.broadcasted_iota(jnp.int32, (tile_side, half_width), 0)
    global_cols = col_id * half_width + lax.broadcasted_iota(jnp.int32, (tile_side, half_width), 1)
    symmetric = jnp.where(global_rows <= global_cols, upper_stored, mirrored)
    near_own = cell_mask(
        block_cells, row_id * tile_blocks, tile_blocks, col_id * half_blocks, half_blocks, NEAR
    )
    far_own = cell_mask(
        block_cells, row_id * tile_blocks, tile_blocks, col_id * half_blocks, half_blocks, FAR
    )
    diagonal = jnp.where(global_rows == global_cols, 0.5, 0.0).astype(jnp.float32)
    value_scale = 2.0 / math.sqrt(order_total)
    density_full = diagonal + value_scale * symmetric.astype(jnp.float32)
    density = jnp.where(near_own, density_full, 0.0).astype(jnp.bfloat16)
    row_panel = lax.all_gather(density, COL, axis=1, tiled=True)
    col_panel_t = column_panel_t(density.T)
    square = jnp.where(far_own, dot_t(row_panel, col_panel_t), 0.0)
    square_low = square.astype(jnp.bfloat16)
    low_panel = lax.all_gather(square_low, COL, axis=1, tiled=True)
    cubic = dot_t(low_panel, col_panel_t)
    return jnp.where(near_own, 3.0 * square - 2.0 * cubic, 0.0).astype(jnp.bfloat16)


def solution(mesh):
    y_size = mesh.devices.shape[0] // 2
    x_size = mesh.devices.shape[1] // 4
    split_mesh = Mesh(mesh.devices.reshape(y_size, 2, 2, x_size, 2), ROW + COL)
    return jax.shard_map(
        per_device,
        mesh=split_mesh,
        in_specs=(P(ROW, COL), P()),
        out_specs=P(ROW, COL),
        check_vma=False,
    )
```

```python
import math

import jax
import jax.numpy as jnp
from jax import lax
from jax.sharding import Mesh
from jax.sharding import PartitionSpec as P

BLK = 64
BOX = 16
NEAR = 40
FAR = 90
ROW = ("y", "zh")
COL = ("zl", "x", "core")
CHUNKS = 1


def cell_mask(block_cells, row_start, row_count, col_start, col_count, bound_sq):
    row_cells = lax.dynamic_slice_in_dim(block_cells, row_start, row_count, 0)
    col_cells = lax.dynamic_slice_in_dim(block_cells, col_start, col_count, 0)
    offset_abs = jnp.abs(row_cells[:, None, :] - col_cells[None, :, :])
    wrapped = jnp.minimum(offset_abs, BOX - offset_abs)
    keep = jnp.sum(wrapped * wrapped, axis=2) <= bound_sq
    return jnp.repeat(jnp.repeat(keep, BLK, axis=0), BLK, axis=1)


def chunked_shift(value, axis, pairs):
    step = value.shape[0] // CHUNKS
    parts = [lax.ppermute(value[i * step:(i + 1) * step], axis, pairs) for i in range(CHUNKS)]
    return jnp.concatenate(parts, 0)


def column_panel_t(tile_t, partner_t):
    zh_id = lax.axis_index("zh")
    pair = jnp.where(zh_id == 0, jnp.concatenate([tile_t, partner_t], 1), jnp.concatenate([partner_t, tile_t], 1))
    ring = lax.axis_size("y")
    up = [(i, (i + 1) % ring) for i in range(ring)]
    down = [(i, (i - 1) % ring) for i in range(ring)]
    from_below = chunked_shift(pair, "y", up)
    from_above = chunked_shift(pair, "y", down)
    from_two_below = chunked_shift(from_below, "y", up)
    y_id = lax.axis_index("y")
    width = pair.shape[1]
    panel = jnp.zeros((pair.shape[0], ring * width), pair.dtype)
    for offset, part in ((0, pair), (-1, from_below), (-2, from_two_below), (1, from_above)):
        panel = lax.dynamic_update_slice_in_dim(panel, part, ((y_id + offset) % ring) * width, 1)
    return panel


def mirror_tiles(upper_stored, rows, cols):
    half_width = upper_stored.shape[1]
    col_id = lax.axis_index(COL)
    h_own = col_id % 2
    mirrors = []
    for row_flip in range(2):
        pieces = []
        for k in range(2):
            half = (col_id + k) % 2
            piece = lax.dynamic_slice_in_dim(upper_stored, half * half_width, half_width, 0)
            pairs = []
            for a in range(rows):
                for b in range(cols):
                    h = (b + k) % 2
                    pairs.append((a * cols + b, ((b // 2) ^ row_flip) * cols + 2 * a + h))
            pieces.append(lax.ppermute(piece, ROW + COL, pairs))
        first = jnp.where(h_own == 0, pieces[0], pieces[1])
        second = jnp.where(h_own == 0, pieces[1], pieces[0])
        mirrors.append(jnp.concatenate([first, second], 1).T)
    return mirrors


def density_tile(upper_stored, mirrored, block_cells, row_id, col_id, order_total):
    tile_side, half_width = upper_stored.shape
    global_rows = row_id * tile_side + lax.broadcasted_iota(jnp.int32, (tile_side, half_width), 0)
    global_cols = col_id * half_width + lax.broadcasted_iota(jnp.int32, (tile_side, half_width), 1)
    symmetric = jnp.where(global_rows <= global_cols, upper_stored, mirrored)
    near = cell_mask(
        block_cells, row_id * (tile_side // BLK), tile_side // BLK,
        col_id * (half_width // BLK), half_width // BLK, NEAR
    )
    diagonal = jnp.where(global_rows == global_cols, 0.5, 0.0).astype(jnp.float32)
    value_scale = 2.0 / math.sqrt(order_total)
    density_full = diagonal + value_scale * symmetric.astype(jnp.float32)
    return jnp.where(near, density_full, 0.0).astype(jnp.bfloat16), near


def dot_t(left, right_t):
    return lax.dot_general(left, right_t, (((1,), (1,)), ((), ())), preferred_element_type=jnp.float32)


def per_device(upper_stored, block_cells):
    rows = lax.axis_size(ROW)
    cols = lax.axis_size(COL)
    row_id = lax.axis_index(ROW)
    col_id = lax.axis_index(COL)
    tile_side, half_width = upper_stored.shape
    order_total = tile_side * rows
    partner_upper = lax.ppermute(upper_stored, "zh", [(0, 1), (1, 0)])
    mirrored, partner_mirrored = mirror_tiles(upper_stored, rows, cols)
    density, near_own = density_tile(upper_stored, mirrored, block_cells, row_id, col_id, order_total)
    partner_density, _ = density_tile(
        partner_upper, partner_mirrored, block_cells, row_id ^ 1, col_id, order_total
    )
    far_own = cell_mask(
        block_cells, row_id * (tile_side // BLK), tile_side // BLK,
        col_id * (half_width // BLK), half_width // BLK, FAR
    )
    row_panel = lax.all_gather(density, COL, axis=1, tiled=True)
    col_panel_t = column_panel_t(density.T, partner_density.T)
    square = jnp.where(far_own, dot_t(row_panel, col_panel_t), 0.0)
    square_low = square.astype(jnp.bfloat16)
    low_panel = lax.all_gather(square_low, COL, axis=1, tiled=True)
    cubic = dot_t(low_panel, col_panel_t)
    return jnp.where(near_own, 3.0 * square - 2.0 * cubic, 0.0).astype(jnp.bfloat16)


def solution(mesh):
    y_size = mesh.devices.shape[0] // 2
    x_size = mesh.devices.shape[1] // 4
    split_mesh = Mesh(mesh.devices.reshape(y_size, 2, 2, x_size, 2), ROW + COL)
    return jax.shard_map(
        per_device,
        mesh=split_mesh,
        in_specs=(P(ROW, COL), P()),
        out_specs=P(ROW, COL),
        check_vma=False,
    )
```

```python
import math

import jax
import jax.numpy as jnp
from jax import lax
from jax.sharding import Mesh
from jax.sharding import PartitionSpec as P

BLK = 64
BOX = 16
NEAR = 40
FAR = 90
ROW = ("y", "zh")
COL = ("zl", "x", "core")
CHUNKS = 1


def cell_mask(block_cells, row_start, row_count, col_start, col_count, bound_sq):
    row_cells = lax.dynamic_slice_in_dim(block_cells, row_start, row_count, 0)
    col_cells = lax.dynamic_slice_in_dim(block_cells, col_start, col_count, 0)
    offset_abs = jnp.abs(row_cells[:, None, :] - col_cells[None, :, :])
    wrapped = jnp.minimum(offset_abs, BOX - offset_abs)
    keep = jnp.sum(wrapped * wrapped, axis=2) <= bound_sq
    return jnp.repeat(jnp.repeat(keep, BLK, axis=0), BLK, axis=1)


def chunked_shift(value, axis, pairs):
    step = value.shape[0] // CHUNKS
    parts = [lax.ppermute(value[i * step:(i + 1) * step], axis, pairs) for i in range(CHUNKS)]
    return jnp.concatenate(parts, 0)


def ring_gather(tile_t, panel, plane):
    ring = lax.axis_size("y")
    up = [(i, (i + 1) % ring) for i in range(ring)]
    down = [(i, (i - 1) % ring) for i in range(ring)]
    from_below = chunked_shift(tile_t, "y", up)
    from_above = chunked_shift(tile_t, "y", down)
    from_two_below = chunked_shift(from_below, "y", up)
    y_id = lax.axis_index("y")
    width = tile_t.shape[1]
    for offset, part in ((0, tile_t), (-1, from_below), (-2, from_two_below), (1, from_above)):
        position = ((y_id + offset) % ring) * 2 + plane
        panel = lax.dynamic_update_slice_in_dim(panel, part, position * width, 1)
    return panel


def column_panel_t(tile_t):
    partner = chunked_shift(tile_t, "zh", [(0, 1), (1, 0)])
    zh_id = lax.axis_index("zh")
    ring = lax.axis_size("y")
    panel = jnp.zeros((tile_t.shape[0], 2 * ring * tile_t.shape[1]), tile_t.dtype)
    panel = ring_gather(tile_t, panel, zh_id)
    return ring_gather(partner, panel, 1 - zh_id)


def mirror_tile(upper_stored, rows, cols):
    tile_side, half_width = upper_stored.shape
    col_id = lax.axis_index(COL)
    pieces = []
    for k in range(2):
        half = (col_id + k) % 2
        piece = lax.dynamic_slice_in_dim(upper_stored, half * half_width, half_width, 0)
        pairs = []
        for a in range(rows):
            for b in range(cols):
                h = (b + k) % 2
                pairs.append((a * cols + b, (b // 2) * cols + 2 * a + h))
        pieces.append(lax.ppermute(piece, ROW + COL, pairs))
    h_own = col_id % 2
    first = jnp.where(h_own == 0, pieces[0], pieces[1])
    second = jnp.where(h_own == 0, pieces[1], pieces[0])
    return jnp.concatenate([first, second], 1).T


def dot_t(left, right_t):
    return lax.dot_general(left, right_t, (((1,), (1,)), ((), ())), preferred_element_type=jnp.float32)


def per_device(upper_stored, block_cells):
    rows = lax.axis_size(ROW)
    cols = lax.axis_size(COL)
    row_id = lax.axis_index(ROW)
    col_id = lax.axis_index(COL)
    tile_side, half_width = upper_stored.shape
    order_total = tile_side * rows
    tile_blocks = tile_side // BLK
    half_blocks = half_width // BLK
    mirrored = mirror_tile(upper_stored, rows, cols)
    global_rows = row_id * tile_side + lax.broadcasted_iota(jnp.int32, (tile_side, half_width), 0)
    global_cols = col_id * half_width + lax.broadcasted_iota(jnp.int32, (tile_side, half_width), 1)
    symmetric = jnp.where(global_rows <= global_cols, upper_stored, mirrored)
    near_own = cell_mask(
        block_cells, row_id * tile_blocks, tile_blocks, col_id * half_blocks, half_blocks, NEAR
    )
    far_own = cell_mask(
        block_cells, row_id * tile_blocks, tile_blocks, col_id * half_blocks, half_blocks, FAR
    )
    diagonal = jnp.where(global_rows == global_cols, 0.5, 0.0).astype(jnp.float32)
    value_scale = 2.0 / math.sqrt(order_total)
    density_full = diagonal + value_scale * symmetric.astype(jnp.float32)
    density = jnp.where(near_own, density_full, 0.0).astype(jnp.bfloat16)
    row_panel = lax.all_gather(density, COL, axis=1, tiled=True)
    col_panel_t = column_panel_t(density.T)
    square = jnp.where(far_own, dot_t(row_panel, col_panel_t), 0.0)
    square_low = square.astype(jnp.bfloat16)
    low_panel = lax.all_gather(square_low, COL, axis=1, tiled=True)
    cubic = dot_t(low_panel, col_panel_t)
    return jnp.where(near_own, 3.0 * square - 2.0 * cubic, 0.0).astype(jnp.bfloat16)


def solution(mesh):
    y_size = mesh.devices.shape[0] // 2
    x_size = mesh.devices.shape[1] // 4
    split_mesh = Mesh(mesh.devices.reshape(y_size, 2, 2, x_size, 2), ROW + COL)
    return jax.shard_map(
        per_device,
        mesh=split_mesh,
        in_specs=(P(ROW, COL), P()),
        out_specs=P(ROW, COL),
        check_vma=False,
    )
```

```python
import math

import jax
import jax.numpy as jnp
from jax import lax
from jax.sharding import Mesh
from jax.sharding import PartitionSpec as P

BLK = 64
BOX = 16
NEAR = 40
FAR = 90
ROW = ("y", "zh")
COL = ("zl", "x", "core")
CHUNKS = 1


def cell_mask(block_cells, row_start, row_count, col_start, col_count, bound_sq):
    row_cells = lax.dynamic_slice_in_dim(block_cells, row_start, row_count, 0)
    col_cells = lax.dynamic_slice_in_dim(block_cells, col_start, col_count, 0)
    offset_abs = jnp.abs(row_cells[:, None, :] - col_cells[None, :, :])
    wrapped = jnp.minimum(offset_abs, BOX - offset_abs)
    keep = jnp.sum(wrapped * wrapped, axis=2) <= bound_sq
    return jnp.repeat(jnp.repeat(keep, BLK, axis=0), BLK, axis=1)


def chunked_shift(value, axis, pairs):
    step = value.shape[0] // CHUNKS
    parts = [lax.ppermute(value[i * step:(i + 1) * step], axis, pairs) for i in range(CHUNKS)]
    return jnp.concatenate(parts, 0)


def ring_gather(tile_t, panel, plane):
    ring = lax.axis_size("y")
    up = [(i, (i + 1) % ring) for i in range(ring)]
    down = [(i, (i - 1) % ring) for i in range(ring)]
    from_below = chunked_shift(tile_t, "y", up)
    from_above = chunked_shift(tile_t, "y", down)
    from_two_below = chunked_shift(from_below, "y", up)
    y_id = lax.axis_index("y")
    width = tile_t.shape[1]
    for offset, part in ((0, tile_t), (-1, from_below), (-2, from_two_below), (1, from_above)):
        position = ((y_id + offset) % ring) * 2 + plane
        panel = lax.dynamic_update_slice_in_dim(panel, part, position * width, 1)
    return panel


def column_panel_t(tile_t):
    partner = chunked_shift(tile_t, "zh", [(0, 1), (1, 0)])
    zh_id = lax.axis_index("zh")
    ring = lax.axis_size("y")
    panel = jnp.zeros((tile_t.shape[0], 2 * ring * tile_t.shape[1]), tile_t.dtype)
    panel = ring_gather(tile_t, panel, zh_id)
    return ring_gather(partner, panel, 1 - zh_id)


def mirror_tile(upper_stored, rows, cols):
    tile_side, half_width = upper_stored.shape
    col_id = lax.axis_index(COL)
    pieces = []
    for k in range(2):
        half = (col_id + k) % 2
        piece = lax.dynamic_slice_in_dim(upper_stored, half * half_width, half_width, 0)
        pairs = []
        for a in range(rows):
            for b in range(cols):
                h = (b + k) % 2
                pairs.append((a * cols + b, (b // 2) * cols + 2 * a + h))
        pieces.append(lax.ppermute(piece, ROW + COL, pairs))
    h_own = col_id % 2
    first = jnp.where(h_own == 0, pieces[0], pieces[1])
    second = jnp.where(h_own == 0, pieces[1], pieces[0])
    return jnp.concatenate([first, second], 1).T


def dot_t(left, right_t):
    return lax.dot_general(left, right_t, (((1,), (1,)), ((), ())), preferred_element_type=jnp.float32)


def per_device(upper_stored, block_cells):
    rows = lax.axis_size(ROW)
    cols = lax.axis_size(COL)
    row_id = lax.axis_index(ROW)
    col_id = lax.axis_index(COL)
    tile_side, half_width = upper_stored.shape
    order_total = tile_side * rows
    tile_blocks = tile_side // BLK
    half_blocks = half_width // BLK
    mirrored = mirror_tile(upper_stored, rows, cols)
    global_rows = row_id * tile_side + lax.broadcasted_iota(jnp.int32, (tile_side, half_width), 0)
    global_cols = col_id * half_width + lax.broadcasted_iota(jnp.int32, (tile_side, half_width), 1)
    symmetric = jnp.where(global_rows <= global_cols, upper_stored, mirrored)
    near_own = cell_mask(
        block_cells, row_id * tile_blocks, tile_blocks, col_id * half_blocks, half_blocks, NEAR
    )
    far_own = cell_mask(
        block_cells, row_id * tile_blocks, tile_blocks, col_id * half_blocks, half_blocks, FAR
    )
    diagonal = jnp.where(global_rows == global_cols, 0.5, 0.0).astype(jnp.float32)
    value_scale = 2.0 / math.sqrt(order_total)
    density_full = diagonal + value_scale * symmetric.astype(jnp.float32)
    density = jnp.where(near_own, density_full, 0.0).astype(jnp.bfloat16)
    row_panel = lax.all_gather(density, COL, axis=1, tiled=True)
    col_panel_t = column_panel_t(density.T)
    half = tile_side // 2
    results = []
    squares = []
    for part in range(2):
        rows_part = slice(part * half, (part + 1) * half)
        squares.append(jnp.where(far_own[rows_part], dot_t(row_panel[rows_part], col_panel_t), 0.0))
    for part in range(2):
        rows_part = slice(part * half, (part + 1) * half)
        low_panel = lax.all_gather(squares[part].astype(jnp.bfloat16), COL, axis=1, tiled=True)
        cubic = dot_t(low_panel, col_panel_t)
        results.append(
            jnp.where(near_own[rows_part], 3.0 * squares[part] - 2.0 * cubic, 0.0).astype(jnp.bfloat16)
        )
    return jnp.concatenate(results, 0)


def solution(mesh):
    y_size = mesh.devices.shape[0] // 2
    x_size = mesh.devices.shape[1] // 4
    split_mesh = Mesh(mesh.devices.reshape(y_size, 2, 2, x_size, 2), ROW + COL)
    return jax.shard_map(
        per_device,
        mesh=split_mesh,
        in_specs=(P(ROW, COL), P()),
        out_specs=P(ROW, COL),
        check_vma=False,
    )
```

```python
import math

import jax
import jax.numpy as jnp
from jax import lax
from jax.sharding import Mesh
from jax.sharding import PartitionSpec as P

BLK = 64
BOX = 16
NEAR = 40
FAR = 90
ROW = ("y", "zh")
COL = ("zl", "x", "core")
CHUNKS = 1


def cell_mask(block_cells, row_start, row_count, col_start, col_count, bound_sq):
    row_cells = lax.dynamic_slice_in_dim(block_cells, row_start, row_count, 0)
    col_cells = lax.dynamic_slice_in_dim(block_cells, col_start, col_count, 0)
    offset_abs = jnp.abs(row_cells[:, None, :] - col_cells[None, :, :])
    wrapped = jnp.minimum(offset_abs, BOX - offset_abs)
    keep = jnp.sum(wrapped * wrapped, axis=2) <= bound_sq
    return jnp.repeat(jnp.repeat(keep, BLK, axis=0), BLK, axis=1)


def chunked_shift(value, axis, pairs):
    step = value.shape[0] // CHUNKS
    parts = [lax.ppermute(value[i * step:(i + 1) * step], axis, pairs) for i in range(CHUNKS)]
    return jnp.concatenate(parts, 0)


def ring_gather(tile_t, panel, plane):
    ring = lax.axis_size("y")
    up = [(i, (i + 1) % ring) for i in range(ring)]
    down = [(i, (i - 1) % ring) for i in range(ring)]
    from_below = chunked_shift(tile_t, "y", up)
    from_above = chunked_shift(tile_t, "y", down)
    from_two_below = chunked_shift(from_below, "y", up)
    y_id = lax.axis_index("y")
    width = tile_t.shape[1]
    for offset, part in ((0, tile_t), (-1, from_below), (-2, from_two_below), (1, from_above)):
        position = ((y_id + offset) % ring) * 2 + plane
        panel = lax.dynamic_update_slice_in_dim(panel, part, position * width, 1)
    return panel


def column_panel_t(tile_t):
    partner = chunked_shift(tile_t, "zh", [(0, 1), (1, 0)])
    zh_id = lax.axis_index("zh")
    ring = lax.axis_size("y")
    panel = jnp.zeros((tile_t.shape[0], 2 * ring * tile_t.shape[1]), tile_t.dtype)
    panel = ring_gather(tile_t, panel, zh_id)
    return ring_gather(partner, panel, 1 - zh_id)


def mirror_tile(upper_stored, rows, cols):
    tile_side, half_width = upper_stored.shape
    col_id = lax.axis_index(COL)
    pieces = []
    for k in range(2):
        half = (col_id + k) % 2
        piece = lax.dynamic_slice_in_dim(upper_stored, half * half_width, half_width, 0)
        pairs = []
        for a in range(rows):
            for b in range(cols):
                h = (b + k) % 2
                pairs.append((a * cols + b, (b // 2) * cols + 2 * a + h))
        pieces.append(lax.ppermute(piece, ROW + COL, pairs))
    h_own = col_id % 2
    first = jnp.where(h_own == 0, pieces[0], pieces[1])
    second = jnp.where(h_own == 0, pieces[1], pieces[0])
    return jnp.concatenate([first, second], 1).T


def plane_panel(tile):
    partner = lax.ppermute(tile, "zl", [(0, 1), (1, 0)])
    zl_id = lax.axis_index("zl")
    pair = jnp.where(zl_id == 0, jnp.concatenate([tile, partner], 1), jnp.concatenate([partner, tile], 1))
    return lax.all_gather(pair, ("x", "core"), axis=1, tiled=True)


def to_plane_order(panel_t, tile_width):
    rows, width = panel_t.shape
    planes = lax.axis_size("zl")
    shaped = panel_t.reshape(rows, planes, width // (planes * tile_width), tile_width)
    return shaped.transpose(0, 2, 1, 3).reshape(rows, width)


def dot_t(left, right_t):
    return lax.dot_general(left, right_t, (((1,), (1,)), ((), ())), preferred_element_type=jnp.float32)


def per_device(upper_stored, block_cells):
    rows = lax.axis_size(ROW)
    cols = lax.axis_size(COL)
    row_id = lax.axis_index(ROW)
    col_id = lax.axis_index(COL)
    tile_side, half_width = upper_stored.shape
    order_total = tile_side * rows
    tile_blocks = tile_side // BLK
    half_blocks = half_width // BLK
    mirrored = mirror_tile(upper_stored, rows, cols)
    global_rows = row_id * tile_side + lax.broadcasted_iota(jnp.int32, (tile_side, half_width), 0)
    global_cols = col_id * half_width + lax.broadcasted_iota(jnp.int32, (tile_side, half_width), 1)
    symmetric = jnp.where(global_rows <= global_cols, upper_stored, mirrored)
    near_own = cell_mask(
        block_cells, row_id * tile_blocks, tile_blocks, col_id * half_blocks, half_blocks, NEAR
    )
    far_own = cell_mask(
        block_cells, row_id * tile_blocks, tile_blocks, col_id * half_blocks, half_blocks, FAR
    )
    diagonal = jnp.where(global_rows == global_cols, 0.5, 0.0).astype(jnp.float32)
    value_scale = 2.0 / math.sqrt(order_total)
    density_full = diagonal + value_scale * symmetric.astype(jnp.float32)
    density = jnp.where(near_own, density_full, 0.0).astype(jnp.bfloat16)
    row_panel = plane_panel(density)
    col_panel_t = to_plane_order(column_panel_t(density.T), half_width)
    square = jnp.where(far_own, dot_t(row_panel, col_panel_t), 0.0)
    square_low = square.astype(jnp.bfloat16)
    low_panel = plane_panel(square_low)
    cubic = dot_t(low_panel, col_panel_t)
    return jnp.where(near_own, 3.0 * square - 2.0 * cubic, 0.0).astype(jnp.bfloat16)


def solution(mesh):
    y_size = mesh.devices.shape[0] // 2
    x_size = mesh.devices.shape[1] // 4
    split_mesh = Mesh(mesh.devices.reshape(y_size, 2, 2, x_size, 2), ROW + COL)
    return jax.shard_map(
        per_device,
        mesh=split_mesh,
        in_specs=(P(ROW, COL), P()),
        out_specs=P(ROW, COL),
        check_vma=False,
    )
```

```python
import math

import jax
import jax.numpy as jnp
from jax import lax
from jax.sharding import Mesh
from jax.sharding import PartitionSpec as P

BLK = 64
BOX = 16
NEAR = 40
FAR = 90
ROW = ("y", "zh")
COL = ("zl", "x", "core")
CHUNKS = 1


def cell_mask(block_cells, row_start, row_count, col_start, col_count, bound_sq):
    row_cells = lax.dynamic_slice_in_dim(block_cells, row_start, row_count, 0)
    col_cells = lax.dynamic_slice_in_dim(block_cells, col_start, col_count, 0)
    offset_abs = jnp.abs(row_cells[:, None, :] - col_cells[None, :, :])
    wrapped = jnp.minimum(offset_abs, BOX - offset_abs)
    keep = jnp.sum(wrapped * wrapped, axis=2) <= bound_sq
    return jnp.repeat(jnp.repeat(keep, BLK, axis=0), BLK, axis=1)


def chunked_shift(value, axis, pairs):
    step = value.shape[0] // CHUNKS
    parts = [lax.ppermute(value[i * step:(i + 1) * step], axis, pairs) for i in range(CHUNKS)]
    return jnp.concatenate(parts, 0)


def ring_gather(tile_t, panel, plane):
    ring = lax.axis_size("y")
    up = [(i, (i + 1) % ring) for i in range(ring)]
    down = [(i, (i - 1) % ring) for i in range(ring)]
    from_below = chunked_shift(tile_t, "y", up)
    from_above = chunked_shift(tile_t, "y", down)
    from_two_below = chunked_shift(from_below, "y", up)
    y_id = lax.axis_index("y")
    width = tile_t.shape[1]
    for offset, part in ((0, tile_t), (-1, from_below), (-2, from_two_below), (1, from_above)):
        position = ((y_id + offset) % ring) * 2 + plane
        panel = lax.dynamic_update_slice_in_dim(panel, part, position * width, 1)
    return panel


def column_panel_t(tile_t):
    partner = chunked_shift(tile_t, "zh", [(0, 1), (1, 0)])
    zh_id = lax.axis_index("zh")
    ring = lax.axis_size("y")
    panel = jnp.zeros((tile_t.shape[0], 2 * ring * tile_t.shape[1]), tile_t.dtype)
    panel = ring_gather(tile_t, panel, zh_id)
    return ring_gather(partner, panel, 1 - zh_id)


def mirror_tile(upper_stored, rows, cols):
    tile_side, half_width = upper_stored.shape
    col_id = lax.axis_index(COL)
    pieces = []
    for k in range(2):
        half = (col_id + k) % 2
        piece = lax.dynamic_slice_in_dim(upper_stored, half * half_width, half_width, 0)
        pairs = []
        for a in range(rows):
            for b in range(cols):
                h = (b + k) % 2
                pairs.append((a * cols + b, (b // 2) * cols + 2 * a + h))
        pieces.append(lax.ppermute(piece, ROW + COL, pairs))
    h_own = col_id % 2
    first = jnp.where(h_own == 0, pieces[0], pieces[1])
    second = jnp.where(h_own == 0, pieces[1], pieces[0])
    return jnp.concatenate([first, second], 1).T


def dot_t(left, right_t):
    return lax.dot_general(left, right_t, (((1,), (1,)), ((), ())), preferred_element_type=jnp.float32)


def per_device(upper_stored, block_cells):
    rows = lax.axis_size(ROW)
    cols = lax.axis_size(COL)
    row_id = lax.axis_index(ROW)
    col_id = lax.axis_index(COL)
    tile_side, half_width = upper_stored.shape
    order_total = tile_side * rows
    tile_blocks = tile_side // BLK
    half_blocks = half_width // BLK
    mirrored = mirror_tile(upper_stored, rows, cols)
    global_rows = row_id * tile_side + lax.broadcasted_iota(jnp.int32, (tile_side, half_width), 0)
    global_cols = col_id * half_width + lax.broadcasted_iota(jnp.int32, (tile_side, half_width), 1)
    symmetric = jnp.where(global_rows <= global_cols, upper_stored, mirrored)
    near_own = cell_mask(
        block_cells, row_id * tile_blocks, tile_blocks, col_id * half_blocks, half_blocks, NEAR
    )
    far_own = cell_mask(
        block_cells, row_id * tile_blocks, tile_blocks, col_id * half_blocks, half_blocks, FAR
    )
    diagonal = jnp.where(global_rows == global_cols, 0.5, 0.0).astype(jnp.float32)
    value_scale = 2.0 / math.sqrt(order_total)
    density_full = diagonal + value_scale * symmetric.astype(jnp.float32)
    density = jnp.where(near_own, density_full, 0.0).astype(jnp.bfloat16)
    core_id = lax.axis_index("core")
    group = ("zl", "x")
    col_panel_t = column_panel_t(density.T)
    by_core = col_panel_t.reshape(half_width, cols // 2, 2, half_width)
    mine = lax.dynamic_index_in_dim(by_core, core_id, 2, keepdims=False).reshape(half_width, -1)
    for_partner = lax.dynamic_index_in_dim(by_core, 1 - core_id, 2, keepdims=False).reshape(half_width, -1)
    from_partner = lax.ppermute(for_partner, "core", [(0, 1), (1, 0)])
    chip_panel_t = jnp.where(
        core_id == 0,
        jnp.concatenate([mine, from_partner], 0),
        jnp.concatenate([from_partner, mine], 0),
    )

    def chip_product(left_tile):
        left = lax.all_gather(left_tile, group, axis=1, tiled=True)
        partial = dot_t(left, chip_panel_t)
        own = jnp.where(core_id == 0, partial[:, :half_width], partial[:, half_width:])
        other = jnp.where(core_id == 0, partial[:, half_width:], partial[:, :half_width])
        return own + lax.ppermute(other, "core", [(0, 1), (1, 0)])

    square = jnp.where(far_own, chip_product(density), 0.0)
    square_low = square.astype(jnp.bfloat16)
    cubic = chip_product(square_low)
    return jnp.where(near_own, 3.0 * square - 2.0 * cubic, 0.0).astype(jnp.bfloat16)


def solution(mesh):
    y_size = mesh.devices.shape[0] // 2
    x_size = mesh.devices.shape[1] // 4
    split_mesh = Mesh(mesh.devices.reshape(y_size, 2, 2, x_size, 2), ROW + COL)
    return jax.shard_map(
        per_device,
        mesh=split_mesh,
        in_specs=(P(ROW, COL), P()),
        out_specs=P(ROW, COL),
        check_vma=False,
    )
```

```python
import math

import jax
import jax.numpy as jnp
from jax import lax
from jax.sharding import Mesh
from jax.sharding import PartitionSpec as P

BLK = 64
BOX = 16
NEAR = 40
FAR = 90
ROW = ("y", "zh")
COL = ("zl", "x", "core")
CHUNKS = 1


def cell_mask(block_cells, row_start, row_count, col_start, col_count, bound_sq):
    row_cells = lax.dynamic_slice_in_dim(block_cells, row_start, row_count, 0)
    col_cells = lax.dynamic_slice_in_dim(block_cells, col_start, col_count, 0)
    offset_abs = jnp.abs(row_cells[:, None, :] - col_cells[None, :, :])
    wrapped = jnp.minimum(offset_abs, BOX - offset_abs)
    keep = jnp.sum(wrapped * wrapped, axis=2) <= bound_sq
    return jnp.repeat(jnp.repeat(keep, BLK, axis=0), BLK, axis=1)


def chunked_shift(value, axis, pairs):
    step = value.shape[0] // CHUNKS
    parts = [lax.ppermute(value[i * step:(i + 1) * step], axis, pairs) for i in range(CHUNKS)]
    return jnp.concatenate(parts, 0)


def ring_gather(tile_t, panel, plane):
    ring = lax.axis_size("y")
    up = [(i, (i + 1) % ring) for i in range(ring)]
    down = [(i, (i - 1) % ring) for i in range(ring)]
    from_below = chunked_shift(tile_t, "y", up)
    from_above = chunked_shift(tile_t, "y", down)
    from_two_below = chunked_shift(from_below, "y", up)
    y_id = lax.axis_index("y")
    width = tile_t.shape[1]
    for offset, part in ((0, tile_t), (-1, from_below), (-2, from_two_below), (1, from_above)):
        position = ((y_id + offset) % ring) * 2 + plane
        panel = lax.dynamic_update_slice_in_dim(panel, part, position * width, 1)
    return panel


def column_panel_t(tile_t):
    partner = chunked_shift(tile_t, "zh", [(0, 1), (1, 0)])
    zh_id = lax.axis_index("zh")
    ring = lax.axis_size("y")
    panel = jnp.zeros((tile_t.shape[0], 2 * ring * tile_t.shape[1]), tile_t.dtype)
    panel = ring_gather(tile_t, panel, zh_id)
    return ring_gather(partner, panel, 1 - zh_id)


def mirror_tile(upper_stored, rows, cols):
    tile_side, half_width = upper_stored.shape
    col_id = lax.axis_index(COL)
    pieces = []
    for k in range(2):
        half = (col_id + k) % 2
        piece = lax.dynamic_slice_in_dim(upper_stored, half * half_width, half_width, 0)
        pairs = []
        for a in range(rows):
            for b in range(cols):
                h = (b + k) % 2
                if a <= b // 2:
                    pairs.append((a * cols + b, (b // 2) * cols + 2 * a + h))
        pieces.append(lax.ppermute(piece, ROW + COL, pairs))
    h_own = col_id % 2
    first = jnp.where(h_own == 0, pieces[0], pieces[1])
    second = jnp.where(h_own == 0, pieces[1], pieces[0])
    return jnp.concatenate([first, second], 1).T


def dot_t(left, right_t):
    return lax.dot_general(left, right_t, (((1,), (1,)), ((), ())), preferred_element_type=jnp.float32)


def per_device(upper_stored, block_cells):
    rows = lax.axis_size(ROW)
    cols = lax.axis_size(COL)
    row_id = lax.axis_index(ROW)
    col_id = lax.axis_index(COL)
    tile_side, half_width = upper_stored.shape
    order_total = tile_side * rows
    tile_blocks = tile_side // BLK
    half_blocks = half_width // BLK
    mirrored = mirror_tile(upper_stored, rows, cols)
    global_rows = row_id * tile_side + lax.broadcasted_iota(jnp.int32, (tile_side, half_width), 0)
    global_cols = col_id * half_width + lax.broadcasted_iota(jnp.int32, (tile_side, half_width), 1)
    symmetric = jnp.where(global_rows <= global_cols, upper_stored, mirrored)
    near_own = cell_mask(
        block_cells, row_id * tile_blocks, tile_blocks, col_id * half_blocks, half_blocks, NEAR
    )
    far_own = cell_mask(
        block_cells, row_id * tile_blocks, tile_blocks, col_id * half_blocks, half_blocks, FAR
    )
    diagonal = jnp.where(global_rows == global_cols, 0.5, 0.0).astype(jnp.float32)
    value_scale = 2.0 / math.sqrt(order_total)
    density_full = diagonal + value_scale * symmetric.astype(jnp.float32)
    density = jnp.where(near_own, density_full, 0.0).astype(jnp.bfloat16)
    row_panel = lax.all_gather(density, COL, axis=1, tiled=True)
    col_panel_t = column_panel_t(density.T)
    square = jnp.where(far_own, dot_t(row_panel, col_panel_t), 0.0)
    square_low = square.astype(jnp.bfloat16)
    low_panel = lax.all_gather(square_low, COL, axis=1, tiled=True)
    cubic = dot_t(low_panel, col_panel_t)
    return jnp.where(near_own, 3.0 * square - 2.0 * cubic, 0.0).astype(jnp.bfloat16)


def solution(mesh):
    y_size = mesh.devices.shape[0] // 2
    x_size = mesh.devices.shape[1] // 4
    split_mesh = Mesh(mesh.devices.reshape(y_size, 2, 2, x_size, 2), ROW + COL)
    return jax.shard_map(
        per_device,
        mesh=split_mesh,
        in_specs=(P(ROW, COL), P()),
        out_specs=P(ROW, COL),
        check_vma=False,
    )
```

```python
import math

import jax
import jax.numpy as jnp
from jax import lax
from jax.sharding import Mesh
from jax.sharding import PartitionSpec as P

BLK = 64
BOX = 16
NEAR = 40
FAR = 90
ROW = ("y", "zh")
COL = ("zl", "x", "core")
CHUNKS = 1


def cell_mask(block_cells, row_start, row_count, col_start, col_count, bound_sq):
    row_cells = lax.dynamic_slice_in_dim(block_cells, row_start, row_count, 0)
    col_cells = lax.dynamic_slice_in_dim(block_cells, col_start, col_count, 0)
    offset_abs = jnp.abs(row_cells[:, None, :] - col_cells[None, :, :])
    wrapped = jnp.minimum(offset_abs, BOX - offset_abs)
    keep = jnp.sum(wrapped * wrapped, axis=2) <= bound_sq
    return jnp.repeat(jnp.repeat(keep, BLK, axis=0), BLK, axis=1)


def chunked_shift(value, axis, pairs):
    step = value.shape[0] // CHUNKS
    parts = [lax.ppermute(value[i * step:(i + 1) * step], axis, pairs) for i in range(CHUNKS)]
    return jnp.concatenate(parts, 0)


def column_panel_t(tile_t):
    ring = lax.axis_size("y")
    y_id = lax.axis_index("y")
    zh_id = lax.axis_index("zh")
    width = tile_t.shape[1]
    panel = jnp.zeros((tile_t.shape[0], 2 * ring * width), tile_t.dtype)
    panel = lax.dynamic_update_slice_in_dim(panel, tile_t, (y_id * 2 + zh_id) * width, 1)
    for dy in range(ring):
        for dz in range(2):
            if dy == 0 and dz == 0:
                continue
            pairs = [
                (y * 2 + z, ((y + dy) % ring) * 2 + (z ^ dz)) for y in range(ring) for z in range(2)
            ]
            part = lax.ppermute(tile_t, ROW, pairs)
            source = ((y_id - dy) % ring) * 2 + (zh_id ^ dz)
            panel = lax.dynamic_update_slice_in_dim(panel, part, source * width, 1)
    return panel


def mirror_tile(upper_stored, rows, cols):
    tile_side, half_width = upper_stored.shape
    col_id = lax.axis_index(COL)
    pieces = []
    for k in range(2):
        half = (col_id + k) % 2
        piece = lax.dynamic_slice_in_dim(upper_stored, half * half_width, half_width, 0)
        pairs = []
        for a in range(rows):
            for b in range(cols):
                h = (b + k) % 2
                if a <= b // 2:
                    pairs.append((a * cols + b, (b // 2) * cols + 2 * a + h))
        pieces.append(lax.ppermute(piece, ROW + COL, pairs))
    h_own = col_id % 2
    first = jnp.where(h_own == 0, pieces[0], pieces[1])
    second = jnp.where(h_own == 0, pieces[1], pieces[0])
    return jnp.concatenate([first, second], 1).T


def dot_t(left, right_t):
    return lax.dot_general(left, right_t, (((1,), (1,)), ((), ())), preferred_element_type=jnp.float32)


def per_device(upper_stored, block_cells):
    rows = lax.axis_size(ROW)
    cols = lax.axis_size(COL)
    row_id = lax.axis_index(ROW)
    col_id = lax.axis_index(COL)
    tile_side, half_width = upper_stored.shape
    order_total = tile_side * rows
    tile_blocks = tile_side // BLK
    half_blocks = half_width // BLK
    mirrored = mirror_tile(upper_stored, rows, cols)
    global_rows = row_id * tile_side + lax.broadcasted_iota(jnp.int32, (tile_side, half_width), 0)
    global_cols = col_id * half_width + lax.broadcasted_iota(jnp.int32, (tile_side, half_width), 1)
    symmetric = jnp.where(global_rows <= global_cols, upper_stored, mirrored)
    near_own = cell_mask(
        block_cells, row_id * tile_blocks, tile_blocks, col_id * half_blocks, half_blocks, NEAR
    )
    far_own = cell_mask(
        block_cells, row_id * tile_blocks, tile_blocks, col_id * half_blocks, half_blocks, FAR
    )
    diagonal = jnp.where(global_rows == global_cols, 0.5, 0.0).astype(jnp.float32)
    value_scale = 2.0 / math.sqrt(order_total)
    density_full = diagonal + value_scale * symmetric.astype(jnp.float32)
    density = jnp.where(near_own, density_full, 0.0).astype(jnp.bfloat16)
    row_panel = lax.all_gather(density, COL, axis=1, tiled=True)
    col_panel_t = column_panel_t(density.T)
    square = jnp.where(far_own, dot_t(row_panel, col_panel_t), 0.0)
    square_low = square.astype(jnp.bfloat16)
    low_panel = lax.all_gather(square_low, COL, axis=1, tiled=True)
    cubic = dot_t(low_panel, col_panel_t)
    return jnp.where(near_own, 3.0 * square - 2.0 * cubic, 0.0).astype(jnp.bfloat16)


def solution(mesh):
    y_size = mesh.devices.shape[0] // 2
    x_size = mesh.devices.shape[1] // 4
    split_mesh = Mesh(mesh.devices.reshape(y_size, 2, 2, x_size, 2), ROW + COL)
    return jax.shard_map(
        per_device,
        mesh=split_mesh,
        in_specs=(P(ROW, COL), P()),
        out_specs=P(ROW, COL),
        check_vma=False,
    )
```

```python
import math

import jax
import jax.numpy as jnp
from jax import lax
from jax.sharding import Mesh
from jax.sharding import PartitionSpec as P

BLK = 64
BOX = 16
NEAR = 40
FAR = 90
ROW = ("y", "zh")
COL = ("zl", "x", "core")
CHUNKS = 1


def cell_mask(block_cells, row_start, row_count, col_start, col_count, bound_sq):
    row_cells = lax.dynamic_slice_in_dim(block_cells, row_start, row_count, 0)
    col_cells = lax.dynamic_slice_in_dim(block_cells, col_start, col_count, 0)
    offset_abs = jnp.abs(row_cells[:, None, :] - col_cells[None, :, :])
    wrapped = jnp.minimum(offset_abs, BOX - offset_abs)
    keep = jnp.sum(wrapped * wrapped, axis=2) <= bound_sq
    return jnp.repeat(jnp.repeat(keep, BLK, axis=0), BLK, axis=1)


def chunked_shift(value, axis, pairs):
    step = value.shape[0] // CHUNKS
    parts = [lax.ppermute(value[i * step:(i + 1) * step], axis, pairs) for i in range(CHUNKS)]
    return jnp.concatenate(parts, 0)


def ring_gather(tile_t, plane, pieces):
    ring = lax.axis_size("y")
    up = [(i, (i + 1) % ring) for i in range(ring)]
    down = [(i, (i - 1) % ring) for i in range(ring)]
    from_below = chunked_shift(tile_t, "y", up)
    from_above = chunked_shift(tile_t, "y", down)
    from_two_below = chunked_shift(from_below, "y", up)
    y_id = lax.axis_index("y")
    for offset, part in ((0, tile_t), (-1, from_below), (1, from_above), (-2, from_two_below)):
        pieces.append((part, ((y_id + offset) % ring) * 2 + plane))


def column_pieces_t(tile_t):
    partner = chunked_shift(tile_t, "zh", [(0, 1), (1, 0)])
    zh_id = lax.axis_index("zh")
    pieces = []
    ring_gather(tile_t, zh_id, pieces)
    ring_gather(partner, 1 - zh_id, pieces)
    return pieces


def assemble(pieces):
    width = pieces[0][0].shape[1]
    panel = jnp.zeros((pieces[0][0].shape[0], len(pieces) * width), pieces[0][0].dtype)
    for part, position in pieces:
        panel = lax.dynamic_update_slice_in_dim(panel, part, position * width, 1)
    return panel


def mirror_tile(upper_stored, rows, cols):
    tile_side, half_width = upper_stored.shape
    col_id = lax.axis_index(COL)
    pieces = []
    for k in range(2):
        half = (col_id + k) % 2
        piece = lax.dynamic_slice_in_dim(upper_stored, half * half_width, half_width, 0)
        pairs = []
        for a in range(rows):
            for b in range(cols):
                h = (b + k) % 2
                if a <= b // 2:
                    pairs.append((a * cols + b, (b // 2) * cols + 2 * a + h))
        pieces.append(lax.ppermute(piece, ROW + COL, pairs))
    h_own = col_id % 2
    first = jnp.where(h_own == 0, pieces[0], pieces[1])
    second = jnp.where(h_own == 0, pieces[1], pieces[0])
    return jnp.concatenate([first, second], 1).T


def dot_t(left, right_t):
    return lax.dot_general(left, right_t, (((1,), (1,)), ((), ())), preferred_element_type=jnp.float32)


def per_device(upper_stored, block_cells):
    rows = lax.axis_size(ROW)
    cols = lax.axis_size(COL)
    row_id = lax.axis_index(ROW)
    col_id = lax.axis_index(COL)
    tile_side, half_width = upper_stored.shape
    order_total = tile_side * rows
    tile_blocks = tile_side // BLK
    half_blocks = half_width // BLK
    mirrored = mirror_tile(upper_stored, rows, cols)
    global_rows = row_id * tile_side + lax.broadcasted_iota(jnp.int32, (tile_side, half_width), 0)
    global_cols = col_id * half_width + lax.broadcasted_iota(jnp.int32, (tile_side, half_width), 1)
    symmetric = jnp.where(global_rows <= global_cols, upper_stored, mirrored)
    near_own = cell_mask(
        block_cells, row_id * tile_blocks, tile_blocks, col_id * half_blocks, half_blocks, NEAR
    )
    far_own = cell_mask(
        block_cells, row_id * tile_blocks, tile_blocks, col_id * half_blocks, half_blocks, FAR
    )
    diagonal = jnp.where(global_rows == global_cols, 0.5, 0.0).astype(jnp.float32)
    value_scale = 2.0 / math.sqrt(order_total)
    density_full = diagonal + value_scale * symmetric.astype(jnp.float32)
    density = jnp.where(near_own, density_full, 0.0).astype(jnp.bfloat16)
    row_panel = lax.all_gather(density, COL, axis=1, tiled=True)
    pieces = column_pieces_t(density.T)
    product = None
    for part, position in pieces:
        term = dot_t(lax.dynamic_slice_in_dim(row_panel, position * tile_side, tile_side, 1), part)
        product = term if product is None else product + term
    square = jnp.where(far_own, product, 0.0)
    col_panel_t = assemble(pieces)
    square_low = square.astype(jnp.bfloat16)
    low_panel = lax.all_gather(square_low, COL, axis=1, tiled=True)
    cubic = dot_t(low_panel, col_panel_t)
    return jnp.where(near_own, 3.0 * square - 2.0 * cubic, 0.0).astype(jnp.bfloat16)


def solution(mesh):
    y_size = mesh.devices.shape[0] // 2
    x_size = mesh.devices.shape[1] // 4
    split_mesh = Mesh(mesh.devices.reshape(y_size, 2, 2, x_size, 2), ROW + COL)
    return jax.shard_map(
        per_device,
        mesh=split_mesh,
        in_specs=(P(ROW, COL), P()),
        out_specs=P(ROW, COL),
        check_vma=False,
    )
```

```python
import math

import jax
import jax.numpy as jnp
from jax import lax
from jax.sharding import Mesh
from jax.sharding import PartitionSpec as P

BLK = 64
BOX = 16
NEAR = 40
FAR = 90
ROW = ("y", "zh")
COL = ("zl", "x", "core")
CHUNKS = 1


def cell_mask(block_cells, row_start, row_count, col_start, col_count, bound_sq):
    row_cells = lax.dynamic_slice_in_dim(block_cells, row_start, row_count, 0)
    col_cells = lax.dynamic_slice_in_dim(block_cells, col_start, col_count, 0)
    offset_abs = jnp.abs(row_cells[:, None, :] - col_cells[None, :, :])
    wrapped = jnp.minimum(offset_abs, BOX - offset_abs)
    keep = jnp.sum(wrapped * wrapped, axis=2) <= bound_sq
    return jnp.repeat(jnp.repeat(keep, BLK, axis=0), BLK, axis=1)


def chunked_shift(value, axis, pairs):
    step = value.shape[0] // CHUNKS
    parts = [lax.ppermute(value[i * step:(i + 1) * step], axis, pairs) for i in range(CHUNKS)]
    return jnp.concatenate(parts, 0)


def ring_gather(tile_t, panel, plane, last=None):
    ring = lax.axis_size("y")
    up = [(i, (i + 1) % ring) for i in range(ring)]
    down = [(i, (i - 1) % ring) for i in range(ring)]
    from_below = chunked_shift(tile_t, "y", up)
    from_above = chunked_shift(tile_t, "y", down)
    from_two_below = chunked_shift(from_below, "y", up)
    y_id = lax.axis_index("y")
    width = tile_t.shape[1]
    for offset, part in ((0, tile_t), (-1, from_below), (-2, from_two_below), (1, from_above)):
        position = ((y_id + offset) % ring) * 2 + plane
        if offset == -2 and last is not None:
            last.append((part, position))
            continue
        panel = lax.dynamic_update_slice_in_dim(panel, part, position * width, 1)
    return panel


def column_panel_t(tile_t):
    partner = chunked_shift(tile_t, "zh", [(0, 1), (1, 0)])
    zh_id = lax.axis_index("zh")
    ring = lax.axis_size("y")
    panel = jnp.zeros((tile_t.shape[0], 2 * ring * tile_t.shape[1]), tile_t.dtype)
    panel = ring_gather(tile_t, panel, zh_id)
    last = []
    panel = ring_gather(partner, panel, 1 - zh_id, last)
    return panel, last[0]


def mirror_tile(upper_stored, rows, cols):
    tile_side, half_width = upper_stored.shape
    col_id = lax.axis_index(COL)
    pieces = []
    for k in range(2):
        half = (col_id + k) % 2
        piece = lax.dynamic_slice_in_dim(upper_stored, half * half_width, half_width, 0)
        pairs = []
        for a in range(rows):
            for b in range(cols):
                h = (b + k) % 2
                if a <= b // 2:
                    pairs.append((a * cols + b, (b // 2) * cols + 2 * a + h))
        pieces.append(lax.ppermute(piece, ROW + COL, pairs))
    h_own = col_id % 2
    first = jnp.where(h_own == 0, pieces[0], pieces[1])
    second = jnp.where(h_own == 0, pieces[1], pieces[0])
    return jnp.concatenate([first, second], 1).T


def dot_t(left, right_t):
    return lax.dot_general(left, right_t, (((1,), (1,)), ((), ())), preferred_element_type=jnp.float32)


def per_device(upper_stored, block_cells):
    rows = lax.axis_size(ROW)
    cols = lax.axis_size(COL)
    row_id = lax.axis_index(ROW)
    col_id = lax.axis_index(COL)
    tile_side, half_width = upper_stored.shape
    order_total = tile_side * rows
    tile_blocks = tile_side // BLK
    half_blocks = half_width // BLK
    mirrored = mirror_tile(upper_stored, rows, cols)
    global_rows = row_id * tile_side + lax.broadcasted_iota(jnp.int32, (tile_side, half_width), 0)
    global_cols = col_id * half_width + lax.broadcasted_iota(jnp.int32, (tile_side, half_width), 1)
    symmetric = jnp.where(global_rows <= global_cols, upper_stored, mirrored)
    near_own = cell_mask(
        block_cells, row_id * tile_blocks, tile_blocks, col_id * half_blocks, half_blocks, NEAR
    )
    far_own = cell_mask(
        block_cells, row_id * tile_blocks, tile_blocks, col_id * half_blocks, half_blocks, FAR
    )
    diagonal = jnp.where(global_rows == global_cols, 0.5, 0.0).astype(jnp.float32)
    value_scale = 2.0 / math.sqrt(order_total)
    density_full = diagonal + value_scale * symmetric.astype(jnp.float32)
    density = jnp.where(near_own, density_full, 0.0).astype(jnp.bfloat16)
    row_panel = lax.all_gather(density, COL, axis=1, tiled=True)
    col_panel_t, (last_t, last_position) = column_panel_t(density.T)

    def product(left):
        left_last = lax.dynamic_slice_in_dim(left, last_position * tile_side, tile_side, 1)
        return dot_t(left, col_panel_t) + dot_t(left_last, last_t)

    square = jnp.where(far_own, product(row_panel), 0.0)
    square_low = square.astype(jnp.bfloat16)
    low_panel = lax.all_gather(square_low, COL, axis=1, tiled=True)
    cubic = product(low_panel)
    return jnp.where(near_own, 3.0 * square - 2.0 * cubic, 0.0).astype(jnp.bfloat16)


def solution(mesh):
    y_size = mesh.devices.shape[0] // 2
    x_size = mesh.devices.shape[1] // 4
    split_mesh = Mesh(mesh.devices.reshape(y_size, 2, 2, x_size, 2), ROW + COL)
    return jax.shard_map(
        per_device,
        mesh=split_mesh,
        in_specs=(P(ROW, COL), P()),
        out_specs=P(ROW, COL),
        check_vma=False,
    )
```

```python
import math

import jax
import jax.numpy as jnp
from jax import lax
from jax.sharding import Mesh
from jax.sharding import PartitionSpec as P

BLK = 64
BOX = 16
NEAR = 40
FAR = 90
ROW = ("y", "zh")
COL = ("zl", "x", "core")
CHUNKS = 1


def cell_mask(block_cells, row_start, row_count, col_start, col_count, bound_sq):
    row_cells = lax.dynamic_slice_in_dim(block_cells, row_start, row_count, 0)
    col_cells = lax.dynamic_slice_in_dim(block_cells, col_start, col_count, 0)
    offset_abs = jnp.abs(row_cells[:, None, :] - col_cells[None, :, :])
    wrapped = jnp.minimum(offset_abs, BOX - offset_abs)
    keep = jnp.sum(wrapped * wrapped, axis=2) <= bound_sq
    return jnp.repeat(jnp.repeat(keep, BLK, axis=0), BLK, axis=1)


def chunked_shift(value, axis, pairs):
    step = value.shape[0] // CHUNKS
    parts = [lax.ppermute(value[i * step:(i + 1) * step], axis, pairs) for i in range(CHUNKS)]
    return jnp.concatenate(parts, 0)


def ring_gather(tile_t, panel, plane):
    ring = lax.axis_size("y")
    up = [(i, (i + 1) % ring) for i in range(ring)]
    down = [(i, (i - 1) % ring) for i in range(ring)]
    from_below = chunked_shift(tile_t, "y", up)
    from_above = chunked_shift(tile_t, "y", down)
    from_two_below = chunked_shift(from_below, "y", up)
    y_id = lax.axis_index("y")
    width = tile_t.shape[1]
    for offset, part in ((0, tile_t), (-1, from_below), (-2, from_two_below), (1, from_above)):
        position = ((y_id + offset) % ring) * 2 + plane
        panel = lax.dynamic_update_slice_in_dim(panel, part, position * width, 1)
    return panel


def column_panel_t(tile_t):
    partner = chunked_shift(tile_t, "zh", [(0, 1), (1, 0)])
    zh_id = lax.axis_index("zh")
    ring = lax.axis_size("y")
    panel = jnp.zeros((tile_t.shape[0], 2 * ring * tile_t.shape[1]), tile_t.dtype)
    panel = ring_gather(tile_t, panel, zh_id)
    return ring_gather(partner, panel, 1 - zh_id)


def mirror_tile(upper_stored, rows, cols):
    half_width = upper_stored.shape[1]
    col_id = lax.axis_index(COL)
    h_own = col_id % 2
    pairs = []
    for a in range(rows):
        for b in range(cols):
            if a <= b // 2:
                pairs.append((a * cols + b, (b // 2) * cols + 2 * a + b % 2))
    received = lax.ppermute(upper_stored, ROW + COL, pairs)
    keep = lax.dynamic_slice_in_dim(received, h_own * half_width, half_width, 0)
    give = lax.dynamic_slice_in_dim(received, (1 - h_own) * half_width, half_width, 0)
    got = lax.ppermute(give, "core", [(0, 1), (1, 0)])
    first = jnp.where(h_own == 0, keep, got)
    second = jnp.where(h_own == 0, got, keep)
    return jnp.concatenate([first, second], 1).T


def dot_t(left, right_t):
    return lax.dot_general(left, right_t, (((1,), (1,)), ((), ())), preferred_element_type=jnp.float32)


def per_device(upper_stored, block_cells):
    rows = lax.axis_size(ROW)
    cols = lax.axis_size(COL)
    row_id = lax.axis_index(ROW)
    col_id = lax.axis_index(COL)
    tile_side, half_width = upper_stored.shape
    order_total = tile_side * rows
    tile_blocks = tile_side // BLK
    half_blocks = half_width // BLK
    mirrored = mirror_tile(upper_stored, rows, cols)
    global_rows = row_id * tile_side + lax.broadcasted_iota(jnp.int32, (tile_side, half_width), 0)
    global_cols = col_id * half_width + lax.broadcasted_iota(jnp.int32, (tile_side, half_width), 1)
    symmetric = jnp.where(global_rows <= global_cols, upper_stored, mirrored)
    near_own = cell_mask(
        block_cells, row_id * tile_blocks, tile_blocks, col_id * half_blocks, half_blocks, NEAR
    )
    far_own = cell_mask(
        block_cells, row_id * tile_blocks, tile_blocks, col_id * half_blocks, half_blocks, FAR
    )
    diagonal = jnp.where(global_rows == global_cols, 0.5, 0.0).astype(jnp.float32)
    value_scale = 2.0 / math.sqrt(order_total)
    density_full = diagonal + value_scale * symmetric.astype(jnp.float32)
    density = jnp.where(near_own, density_full, 0.0).astype(jnp.bfloat16)
    row_panel = lax.all_gather(density, COL, axis=1, tiled=True)
    col_panel_t = column_panel_t(density.T)
    square = jnp.where(far_own, dot_t(row_panel, col_panel_t), 0.0)
    square_low = square.astype(jnp.bfloat16)
    low_panel = lax.all_gather(square_low, COL, axis=1, tiled=True)
    cubic = dot_t(low_panel, col_panel_t)
    return jnp.where(near_own, 3.0 * square - 2.0 * cubic, 0.0).astype(jnp.bfloat16)


def solution(mesh):
    y_size = mesh.devices.shape[0] // 2
    x_size = mesh.devices.shape[1] // 4
    split_mesh = Mesh(mesh.devices.reshape(y_size, 2, 2, x_size, 2), ROW + COL)
    return jax.shard_map(
        per_device,
        mesh=split_mesh,
        in_specs=(P(ROW, COL), P()),
        out_specs=P(ROW, COL),
        check_vma=False,
    )
```

```python
import math

import jax
import jax.numpy as jnp
from jax import lax
from jax.sharding import Mesh
from jax.sharding import PartitionSpec as P


BLK = 64
BOX = 16
NEAR = 40
FAR = 90
ROW = ("y", "zh")
COL = ("zl", "x", "core")


def cell_mask(block_cells, row_start, row_count, col_start, col_count, bound_sq):
    row_cells = lax.dynamic_slice_in_dim(block_cells, row_start, row_count, 0)
    col_cells = lax.dynamic_slice_in_dim(block_cells, col_start, col_count, 0)
    offset_abs = jnp.abs(row_cells[:, None, :] - col_cells[None, :, :])
    wrapped = jnp.minimum(offset_abs, BOX - offset_abs)
    keep = jnp.sum(wrapped * wrapped, axis=2) <= bound_sq
    return jnp.repeat(jnp.repeat(keep, BLK, axis=0), BLK, axis=1)


def column_panel_t(tile_t):
    ring = lax.axis_size("y")
    y_id = lax.axis_index("y")
    zh_id = lax.axis_index("zh")
    width = tile_t.shape[1]
    panel = jnp.zeros((tile_t.shape[0], 2 * ring * width), tile_t.dtype)

    def send(value, dy, dz):
        pairs = [(y * 2 + z, ((y + dy) % ring) * 2 + (z ^ dz)) for y in range(ring) for z in range(2)]
        return lax.ppermute(value, ROW, pairs)

    partner = send(tile_t, 0, 1)
    received = [(1, 0, send(tile_t, 1, 0)), (-1, 0, send(tile_t, -1, 0)), (2, 0, send(tile_t, 2, 0)),
                (2, 1, send(tile_t, 2, 1)), (0, 1, partner)]
    received += [(1, 1, send(partner, 1, 0)), (-1, 1, send(partner, -1, 0))]
    for dy, dz, part in received:
        source = ((y_id - dy) % ring) * 2 + (zh_id ^ dz)
        panel = lax.dynamic_update_slice_in_dim(panel, part, source * width, 1)
    return lax.dynamic_update_slice_in_dim(panel, tile_t, (y_id * 2 + zh_id) * width, 1)


def mirror_tile(upper_stored, rows, cols):
    _, half_width = upper_stored.shape
    col_id = lax.axis_index(COL)
    pieces = []
    for k in range(2):
        half = (col_id + k) % 2
        piece = lax.dynamic_slice_in_dim(upper_stored, half * half_width, half_width, 0)
        pairs = []
        for a in range(rows):
            for b in range(cols):
                h = (b + k) % 2
                if a <= b // 2:
                    pairs.append((a * cols + b, (b // 2) * cols + 2 * a + h))
        pieces.append(lax.ppermute(piece, ROW + COL, pairs))
    h_own = col_id % 2
    first = jnp.where(h_own == 0, pieces[0], pieces[1])
    second = jnp.where(h_own == 0, pieces[1], pieces[0])
    return jnp.concatenate([first, second], 1).T


def dot_t(left, right_t):
    return lax.dot_general(left, right_t, (((1,), (1,)), ((), ())), preferred_element_type=jnp.float32)


def per_device_body(upper_stored, block_cells):
    rows = lax.axis_size(ROW)
    cols = lax.axis_size(COL)
    row_id = lax.axis_index(ROW)
    col_id = lax.axis_index(COL)
    tile_side, half_width = upper_stored.shape
    order_total = tile_side * rows
    tile_blocks = tile_side // BLK
    half_blocks = half_width // BLK
    mirrored = mirror_tile(upper_stored, rows, cols)
    global_rows = row_id * tile_side + lax.broadcasted_iota(jnp.int32, (tile_side, half_width), 0)
    global_cols = col_id * half_width + lax.broadcasted_iota(jnp.int32, (tile_side, half_width), 1)
    symmetric = jnp.where(global_rows <= global_cols, upper_stored, mirrored)
    near_own = cell_mask(
        block_cells, row_id * tile_blocks, tile_blocks, col_id * half_blocks, half_blocks, NEAR
    )
    far_own = cell_mask(
        block_cells, row_id * tile_blocks, tile_blocks, col_id * half_blocks, half_blocks, FAR
    )
    diagonal = jnp.where(global_rows == global_cols, 0.5, 0.0).astype(jnp.float32)
    value_scale = 2.0 / math.sqrt(order_total)
    density_full = diagonal + value_scale * symmetric.astype(jnp.float32)
    density = jnp.where(near_own, density_full, 0.0).astype(jnp.bfloat16)
    row_panel = lax.all_gather(density, COL, axis=1, tiled=True)
    col_panel_t = column_panel_t(density.T)
    square = jnp.where(far_own, dot_t(row_panel, col_panel_t), 0.0)
    square_low = square.astype(jnp.bfloat16)
    low_panel = lax.all_gather(square_low, COL, axis=1, tiled=True)
    cubic = dot_t(low_panel, col_panel_t)
    return jnp.where(near_own, 3.0 * square - 2.0 * cubic, 0.0).astype(jnp.bfloat16)


def solution(mesh):
    y_size = mesh.devices.shape[0] // 2
    x_size = mesh.devices.shape[1] // 4
    split_mesh = Mesh(mesh.devices.reshape(y_size, 2, 2, x_size, 2), ROW + COL)
    return jax.shard_map(
        per_device_body,
        mesh=split_mesh,
        in_specs=(P(ROW, COL), P()),
        out_specs=P(ROW, COL),
        check_vma=False,
    )
```

```python
import math

import jax
import jax.numpy as jnp
from jax import lax
from jax.sharding import Mesh
from jax.sharding import PartitionSpec as P


BLK = 64
BOX = 16
NEAR = 40
FAR = 90
ROW = ("y", "zh")
COL = ("zl", "x", "core")
CHUNKS = 1


def cell_mask(block_cells, row_start, row_count, col_start, col_count, bound_sq):
    row_cells = lax.dynamic_slice_in_dim(block_cells, row_start, row_count, 0)
    col_cells = lax.dynamic_slice_in_dim(block_cells, col_start, col_count, 0)
    offset_abs = jnp.abs(row_cells[:, None, :] - col_cells[None, :, :])
    wrapped = jnp.minimum(offset_abs, BOX - offset_abs)
    keep = jnp.sum(wrapped * wrapped, axis=2) <= bound_sq
    return jnp.repeat(jnp.repeat(keep, BLK, axis=0), BLK, axis=1)


def chunked_shift(value, axis, pairs):
    step = value.shape[0] // CHUNKS
    parts = [lax.ppermute(value[i * step:(i + 1) * step], axis, pairs) for i in range(CHUNKS)]
    return jnp.concatenate(parts, 0)


def ring_gather(tile_t, panel, plane):
    ring = lax.axis_size("y")
    up = [(i, (i + 1) % ring) for i in range(ring)]
    down = [(i, (i - 1) % ring) for i in range(ring)]
    from_below = chunked_shift(tile_t, "y", up)
    from_above = chunked_shift(tile_t, "y", down)
    from_two_below = chunked_shift(from_below, "y", up)
    y_id = lax.axis_index("y")
    width = tile_t.shape[1]
    for offset, part in ((0, tile_t), (-1, from_below), (-2, from_two_below), (1, from_above)):
        position = ((y_id + offset) % ring) * 2 + plane
        panel = lax.dynamic_update_slice_in_dim(panel, part, position * width, 1)
    return panel


def column_panel_t(tile_t):
    partner = chunked_shift(tile_t, "zh", [(0, 1), (1, 0)])
    zh_id = lax.axis_index("zh")
    ring = lax.axis_size("y")
    panel = jnp.zeros((tile_t.shape[0], 2 * ring * tile_t.shape[1]), tile_t.dtype)
    panel = ring_gather(tile_t, panel, zh_id)
    return ring_gather(partner, panel, 1 - zh_id)


def mirror_tile(upper_stored, rows, cols):
    _, half_width = upper_stored.shape
    col_id = lax.axis_index(COL)
    pieces = []
    for k in range(2):
        half = (col_id + k) % 2
        piece = lax.dynamic_slice_in_dim(upper_stored, half * half_width, half_width, 0)
        pairs = []
        for a in range(rows):
            for b in range(cols):
                h = (b + k) % 2
                if a <= b // 2:
                    pairs.append((a * cols + b, (b // 2) * cols + 2 * a + h))
        pieces.append(lax.ppermute(piece, ROW + COL, pairs))
    h_own = col_id % 2
    first = jnp.where(h_own == 0, pieces[0], pieces[1])
    second = jnp.where(h_own == 0, pieces[1], pieces[0])
    return jnp.concatenate([first, second], 1).T


GATHER_ORDER = ("core", "zl", "x")


def to_gather_order(panel_t, block):
    rows, width = panel_t.shape
    x_size = width // (4 * block)
    shaped = panel_t.reshape(rows, 2, x_size, 2, block)
    return shaped.transpose(0, 3, 1, 2, 4).reshape(rows, width)


def dot_t(left, right_t):
    return lax.dot_general(left, right_t, (((1,), (1,)), ((), ())), preferred_element_type=jnp.float32)


def per_device_body(upper_stored, block_cells):
    rows = lax.axis_size(ROW)
    cols = lax.axis_size(COL)
    row_id = lax.axis_index(ROW)
    col_id = lax.axis_index(COL)
    tile_side, half_width = upper_stored.shape
    order_total = tile_side * rows
    tile_blocks = tile_side // BLK
    half_blocks = half_width // BLK
    mirrored = mirror_tile(upper_stored, rows, cols)
    global_rows = row_id * tile_side + lax.broadcasted_iota(jnp.int32, (tile_side, half_width), 0)
    global_cols = col_id * half_width + lax.broadcasted_iota(jnp.int32, (tile_side, half_width), 1)
    symmetric = jnp.where(global_rows <= global_cols, upper_stored, mirrored)
    near_own = cell_mask(
        block_cells, row_id * tile_blocks, tile_blocks, col_id * half_blocks, half_blocks, NEAR
    )
    far_own = cell_mask(
        block_cells, row_id * tile_blocks, tile_blocks, col_id * half_blocks, half_blocks, FAR
    )
    diagonal = jnp.where(global_rows == global_cols, 0.5, 0.0).astype(jnp.float32)
    value_scale = 2.0 / math.sqrt(order_total)
    density_full = diagonal + value_scale * symmetric.astype(jnp.float32)
    density = jnp.where(near_own, density_full, 0.0).astype(jnp.bfloat16)
    row_panel = lax.all_gather(density, GATHER_ORDER, axis=1, tiled=True)
    col_panel_t = column_panel_t(density.T)
    col_panel_t = to_gather_order(col_panel_t, half_width)
    square = jnp.where(far_own, dot_t(row_panel, col_panel_t), 0.0)
    square_low = square.astype(jnp.bfloat16)
    low_panel = lax.all_gather(square_low, GATHER_ORDER, axis=1, tiled=True)
    cubic = dot_t(low_panel, col_panel_t)
    return jnp.where(near_own, 3.0 * square - 2.0 * cubic, 0.0).astype(jnp.bfloat16)


def solution(mesh):
    y_size = mesh.devices.shape[0] // 2
    x_size = mesh.devices.shape[1] // 4
    split_mesh = Mesh(mesh.devices.reshape(y_size, 2, 2, x_size, 2), ROW + COL)
    return jax.shard_map(
        per_device_body,
        mesh=split_mesh,
        in_specs=(P(ROW, COL), P()),
        out_specs=P(ROW, COL),
        check_vma=False,
    )
```

```python
import math

import jax
import jax.numpy as jnp
from jax import lax
from jax.sharding import Mesh
from jax.sharding import PartitionSpec as P


BLK = 64
BOX = 16
NEAR = 40
FAR = 90
ROW = ("y", "zh")
COL = ("zl", "x", "core")
CHUNKS = 1


def cell_mask(block_cells, row_start, row_count, col_start, col_count, bound_sq):
    row_cells = lax.dynamic_slice_in_dim(block_cells, row_start, row_count, 0)
    col_cells = lax.dynamic_slice_in_dim(block_cells, col_start, col_count, 0)
    offset_abs = jnp.abs(row_cells[:, None, :] - col_cells[None, :, :])
    wrapped = jnp.minimum(offset_abs, BOX - offset_abs)
    keep = jnp.sum(wrapped * wrapped, axis=2) <= bound_sq
    return jnp.repeat(jnp.repeat(keep, BLK, axis=0), BLK, axis=1)


def chunked_shift(value, axis, pairs):
    step = value.shape[0] // CHUNKS
    parts = [lax.ppermute(value[i * step:(i + 1) * step], axis, pairs) for i in range(CHUNKS)]
    return jnp.concatenate(parts, 0)


def ring_gather(tile_t, panel, plane):
    ring = lax.axis_size("y")
    up = [(i, (i + 1) % ring) for i in range(ring)]
    down = [(i, (i - 1) % ring) for i in range(ring)]
    from_below = chunked_shift(tile_t, "y", up)
    from_above = chunked_shift(tile_t, "y", down)
    from_two_below = chunked_shift(from_below, "y", up)
    y_id = lax.axis_index("y")
    width = tile_t.shape[1]
    for offset, part in ((0, tile_t), (-1, from_below), (-2, from_two_below), (1, from_above)):
        position = ((y_id + offset) % ring) * 2 + plane
        panel = lax.dynamic_update_slice_in_dim(panel, part, position * width, 1)
    return panel


def column_panel_t(tile_t):
    partner = chunked_shift(tile_t, "zh", [(0, 1), (1, 0)])
    zh_id = lax.axis_index("zh")
    ring = lax.axis_size("y")
    panel = jnp.zeros((tile_t.shape[0], 2 * ring * tile_t.shape[1]), tile_t.dtype)
    panel = ring_gather(tile_t, panel, zh_id)
    return ring_gather(partner, panel, 1 - zh_id)


def mirror_tile(upper_stored, rows, cols):
    _, half_width = upper_stored.shape
    col_id = lax.axis_index(COL)
    pieces = []
    for k in range(2):
        half = (col_id + k) % 2
        piece = lax.dynamic_slice_in_dim(upper_stored, half * half_width, half_width, 0)
        pairs = []
        for a in range(rows):
            for b in range(cols):
                h = (b + k) % 2
                if a <= b // 2:
                    pairs.append((a * cols + b, (b // 2) * cols + 2 * a + h))
        pieces.append(lax.ppermute(piece, ROW + COL, pairs))
    h_own = col_id % 2
    first = jnp.where(h_own == 0, pieces[0], pieces[1])
    second = jnp.where(h_own == 0, pieces[1], pieces[0])
    return jnp.concatenate([first, second], 1).T


def dot_t(left, right_t):
    return lax.dot_general(left, right_t, (((1,), (1,)), ((), ())), preferred_element_type=jnp.float32)


def per_device_body(upper_stored, block_cells):
    rows = lax.axis_size(ROW)
    cols = lax.axis_size(COL)
    row_id = lax.axis_index(ROW)
    col_id = lax.axis_index(COL)
    tile_side, half_width = upper_stored.shape
    order_total = tile_side * rows
    tile_blocks = tile_side // BLK
    half_blocks = half_width // BLK
    mirrored = mirror_tile(upper_stored, rows, cols)
    global_rows = row_id * tile_side + lax.broadcasted_iota(jnp.int32, (tile_side, half_width), 0)
    global_cols = col_id * half_width + lax.broadcasted_iota(jnp.int32, (tile_side, half_width), 1)
    symmetric = jnp.where(global_rows <= global_cols, upper_stored, mirrored)
    near_own = cell_mask(
        block_cells, row_id * tile_blocks, tile_blocks, col_id * half_blocks, half_blocks, NEAR
    )
    far_own = cell_mask(
        block_cells, row_id * tile_blocks, tile_blocks, col_id * half_blocks, half_blocks, FAR
    )
    diagonal = jnp.where(global_rows == global_cols, 0.5, 0.0).astype(jnp.float32)
    value_scale = 2.0 / math.sqrt(order_total)
    density_full = diagonal + value_scale * symmetric.astype(jnp.float32)
    density = jnp.where(near_own, density_full, 0.0).astype(jnp.bfloat16)
    row_panel = lax.all_gather(density, COL, axis=1, tiled=True)
    col_panel_t = column_panel_t(density.T)
    square = jnp.where(far_own, dot_t(row_panel, col_panel_t), 0.0)
    square_low = square.astype(jnp.bfloat16)
    low_panel = lax.all_gather(square_low, COL, axis=1, tiled=True)
    cubic = dot_t(low_panel, col_panel_t)
    return jnp.where(near_own, 3.0 * square - 2.0 * cubic, 0.0).astype(jnp.bfloat16)


def solution(mesh):
    y_size = mesh.devices.shape[0] // 2
    x_size = mesh.devices.shape[1] // 4
    split_mesh = Mesh(mesh.devices.reshape(y_size, 2, 2, x_size, 2), ROW + COL)
    return jax.shard_map(
        per_device_body,
        mesh=split_mesh,
        in_specs=(P(ROW, COL), P()),
        out_specs=P(ROW, COL),
        check_vma=False,
    )
```
